256 devices in a mesh: section: 8 (over y_lo, x), expert: 32 (over z, y_hi, core).
Axes of the slice: x: 4, y: 4 (y_hi: 2, y_lo: 2; y = y_hi * 2 + y_lo), z: 8, core: 2. Of those that a mesh axis runs over, the one named last changes fastest.
Arguments:
- tokens: bfloat16 [32768, 4096], P(('section', 'expert')), may hold values from -6 to 6
- expert_ids: int32 [32768], P(('section', 'expert')), may hold values from 0 to 31, as said below
- slot_ids: int32 [32768], P(('section', 'expert')), may hold values from 0 to 4, as said below
- router: bfloat16 [4096, 32], replicated, may hold values from -0.09375 to 0.09375
- w_in: bfloat16 [32, 4096, 5120], P('expert', None, 'section'), may hold values from -0.09375 to 0.09375
- w_out: bfloat16 [32, 5120, 4096], P('expert', 'section'), may hold values from -0.078125 to 0.078125
Outputs:
- moe_out: bfloat16 [32768, 4096], P(('section', 'expert'))
The draws below stay inside these ranges and needn't reach their ends.
Inputs may be any that keep to these rules, and one draw needn't show every extreme that they name: `expert_ids`: within each aligned block of 128 rows (the tokens of one device) no pair of expert id and slot position occurs twice, so each expert receives at most 5 tokens from one device. `slot_ids`: a token's position among the 5 slots that its device keeps for its expert.
All inputs are finite; a program needn't handle non-finite values.
Results may differ from the reference program's by a relative error of at most 0.018.
Values may be sent and summed in bfloat16 or wider, within the bound.
No kernel may reach another device: no remote copies, remote signals or barrier semaphores. Data moves between devices by JAX's collectives and lax.ppermute only.
A program may use at most 128 MiB of HBM per device.

```python
import jax
import jax.numpy as jnp
from jax import lax

D = 4096
FF = 5120
TOK_DEV = 128
EXPERTS = 32
CAP = 5
TOKENS = 32768
N_SECTION = 8


def routing_cells(key):
    base_key = jax.random.fold_in(key, 11)
    block_count = TOKENS // TOK_DEV
    cell_count = EXPERTS * CAP
    full_expert = jax.random.randint(jax.random.fold_in(base_key, 3), (), 0, EXPERTS)

    def draw_block(block_index):
        block_key = jax.random.fold_in(base_key, block_index + 100)
        score_key, order_key = jax.random.split(block_key)
        scores = jax.random.randint(score_key, (cell_count,), 0, 65536) * cell_count + jnp.arange(cell_count, dtype=jnp.int32)
        owners = jnp.arange(cell_count, dtype=jnp.int32) // CAP
        scores = jnp.where(owners == full_expert, scores + 268435456, scores)
        taken = lax.top_k(scores, TOK_DEV)[1]
        return jax.random.permutation(order_key, taken)
    chosen = jax.vmap(draw_block)(jnp.arange(block_count, dtype=jnp.int32))
    return chosen.reshape(-1).astype(jnp.int32)


def draw_expert_ids(key, part):
    return (routing_cells(key) // CAP).astype(jnp.int32)


def draw_slot_ids(key, part):
    return (routing_cells(key) % CAP).astype(jnp.int32)


def block_levels(stream_key, extent, cuts, least, largest):
    gain = 1.0
    for dim, parts in cuts:
        heights = jax.random.uniform(jax.random.fold_in(jax.random.fold_in(stream_key, 6), dim), (parts,), jnp.float32, least / len(cuts), largest / len(cuts))
        gain = gain * jnp.repeat(jnp.exp(heights), extent[dim] // parts).reshape((-1,) + (1,) * (len(extent) - 1 - dim))
    return gain


def bell_draw(own_key, extent, deviation, most, shards=(), kind=jnp.bfloat16):
    drawn = jax.random.normal(own_key, extent, jnp.float32) * deviation
    if len(shards) > 0:
        drawn = block_levels(own_key, extent, shards, -0.22, 0.18) * drawn
    return jnp.clip(drawn, min=-most, max=most).astype(kind)


def setup_inputs(seed: int = 0) -> dict:
    seeds = jax.random.split(jax.random.key(seed), 7)
    return {
        "tokens": bell_draw(seeds[0], (TOKENS, D), 1.0, 6.0, ((0, 256),)),
        "expert_ids": draw_expert_ids(jax.random.fold_in(seeds[6], 71), 0),
        "slot_ids": draw_slot_ids(jax.random.fold_in(seeds[6], 71), 0),
        "router": bell_draw(seeds[3], (D, EXPERTS), D ** -0.5, 0.09375),
        "w_in": bell_draw(seeds[4], (EXPERTS, D, FF), D ** -0.5, 0.09375, ((0, 32), (2, 8))),
        "w_out": bell_draw(seeds[5], (EXPERTS, FF, D), FF ** -0.5, 0.078125, ((0, 32), (1, 8))),
    }


def reference(tokens, expert_ids, slot_ids, router, w_in, w_out):
    tok_total = tokens.shape[0]
    block_count = tok_total // TOK_DEV
    group_width = FF // N_SECTION
    logits = jnp.dot(tokens, router, preferred_element_type=jnp.float32)
    chosen = expert_ids[:, None] == jnp.arange(EXPERTS, dtype=jnp.int32)[None, :]
    gating = jax.nn.sigmoid(jnp.sum(jnp.where(chosen, logits, jnp.zeros_like(logits)), axis=1))
    block_of = (jnp.arange(tok_total, dtype=jnp.int32) // TOK_DEV).astype(jnp.int32)
    position = ((expert_ids * block_count + block_of) * CAP + slot_ids).astype(jnp.int32)
    slot_table = jnp.zeros((EXPERTS * block_count * CAP, D), jnp.bfloat16).at[position].set(tokens)
    slot_table = slot_table.reshape(EXPERTS, block_count * CAP, D)

    def expert_ffn(operands):
        slot_rows, inward, outward = operands
        hidden = jax.nn.relu(jnp.dot(slot_rows, inward, preferred_element_type=jnp.float32)).astype(jnp.bfloat16)
        hidden = lax.optimization_barrier(hidden)
        grouped = hidden.reshape(slot_rows.shape[0], N_SECTION, group_width).astype(jnp.float32)
        out_groups = outward.reshape(N_SECTION, group_width, D).astype(jnp.float32)
        partial_value = jnp.einsum("rgf,gfd->grd", grouped, out_groups).astype(jnp.bfloat16)
        partial_value = lax.optimization_barrier(partial_value)
        return jnp.sum(partial_value.astype(jnp.float32), axis=0).astype(jnp.bfloat16)

    expert_out = lax.map(expert_ffn, (slot_table, w_in, w_out))
    picked = expert_out.reshape(-1, D)[position]
    return (gating[:, None] * picked.astype(jnp.float32)).astype(jnp.bfloat16)
```

```python
import jax
import jax.numpy as jnp
from jax import lax
from jax.sharding import PartitionSpec as P


def per_device(tokens, expert_ids, slot_ids, router, w_in, w_out):
    tok_rows, width_model = tokens.shape
    experts = router.shape[1]
    capacity = 5 * tok_rows // (4 * experts)
    cell_index = expert_ids * capacity + slot_ids
    onehot = (
        cell_index[None, :] == jnp.arange(experts * capacity, dtype=jnp.int32)[:, None]
    ).astype(jnp.bfloat16)
    dispatch = jnp.dot(onehot, tokens, preferred_element_type=jnp.float32).astype(jnp.bfloat16)
    dispatch = dispatch.reshape(1, experts, capacity, width_model)
    inward = w_in[0]
    outward = w_out[0]
    routed = lax.all_to_all(dispatch[0], "expert", split_axis=0, concat_axis=0, tiled=True)
    arrived = lax.all_gather(routed, "section", axis=0, tiled=True)
    flat = arrived.reshape(-1, width_model)
    hidden = jax.nn.relu(jnp.dot(flat, inward, preferred_element_type=jnp.float32)).astype(
        jnp.bfloat16
    )
    summed = lax.psum_scatter(
        jnp.dot(hidden, outward, preferred_element_type=jnp.float32).astype(jnp.bfloat16),
        "section",
        scatter_dimension=0,
        tiled=True,
    )
    expert_out = summed.reshape(experts, capacity, width_model)
    returned = lax.all_to_all(expert_out, "expert", split_axis=0, concat_axis=0, tiled=True)
    combined = lax.dot_general(
        onehot,
        returned.reshape(-1, width_model),
        (((0,), (0,)), ((), ())),
        preferred_element_type=jnp.float32,
    )
    logits = jnp.dot(tokens, router, preferred_element_type=jnp.float32)
    chosen = expert_ids[:, None] == jnp.arange(experts, dtype=jnp.int32)[None, :]
    gating = jax.nn.sigmoid(jnp.sum(jnp.where(chosen, logits, jnp.zeros_like(logits)), axis=1))
    return (gating[:, None] * combined).astype(jnp.bfloat16)


def solution(mesh):
    return jax.shard_map(
        per_device,
        mesh=mesh,
        in_specs=(
            P(("section", "expert"), None),
            P(("section", "expert")),
            P(("section", "expert")),
            P(),
            P("expert", None, "section"),
            P("expert", "section", None),
        ),
        out_specs=P(("section", "expert"), None),
        check_vma=False,
    )
```

```python
import jax
import jax.numpy as jnp
from jax import lax
from jax.sharding import PartitionSpec as P

CHUNK_SLOTS = (1, 1, 1, 1, 1)


def per_device(tokens, expert_ids, slot_ids, router, w_in, w_out):
    tok_rows, width_model = tokens.shape
    experts = router.shape[1]
    capacity = 5 * tok_rows // (4 * experts)
    assert sum(CHUNK_SLOTS) == capacity
    cell_index = slot_ids * experts + expert_ids
    onehot = (
        cell_index[None, :] == jnp.arange(experts * capacity, dtype=jnp.int32)[:, None]
    ).astype(jnp.bfloat16)
    dispatch = jnp.dot(onehot, tokens, preferred_element_type=jnp.float32).astype(jnp.bfloat16)
    inward = w_in[0]
    outward = w_out[0]

    combined = None
    start = 0
    for slots in CHUNK_SLOTS:
        rows = slice(start * experts, (start + slots) * experts)
        start += slots
        part = dispatch[rows].reshape(slots, experts, width_model)
        routed = lax.all_to_all(part, "expert", split_axis=1, concat_axis=1, tiled=True)
        arrived = lax.all_gather(
            routed.reshape(-1, width_model), "section", axis=0, tiled=True
        )
        hidden = jax.nn.relu(
            jnp.dot(arrived, inward, preferred_element_type=jnp.float32)
        ).astype(jnp.bfloat16)
        summed = lax.psum_scatter(
            jnp.dot(hidden, outward, preferred_element_type=jnp.float32).astype(jnp.bfloat16),
            "section",
            scatter_dimension=0,
            tiled=True,
        )
        returned = lax.all_to_all(
            summed.reshape(slots, experts, width_model),
            "expert",
            split_axis=1,
            concat_axis=1,
            tiled=True,
        )
        piece = lax.dot_general(
            onehot[rows],
            returned.reshape(-1, width_model),
            (((0,), (0,)), ((), ())),
            preferred_element_type=jnp.float32,
        )
        combined = piece if combined is None else combined + piece
    logits = jnp.dot(tokens, router, preferred_element_type=jnp.float32)
    chosen = expert_ids[:, None] == jnp.arange(experts, dtype=jnp.int32)[None, :]
    gating = jax.nn.sigmoid(jnp.sum(jnp.where(chosen, logits, jnp.zeros_like(logits)), axis=1))
    return (gating[:, None] * combined).astype(jnp.bfloat16)


def solution(mesh):
    return jax.shard_map(
        per_device,
        mesh=mesh,
        in_specs=(
            P(("section", "expert"), None),
            P(("section", "expert")),
            P(("section", "expert")),
            P(),
            P("expert", None, "section"),
            P("expert", "section", None),
        ),
        out_specs=P(("section", "expert"), None),
        check_vma=False,
    )
```

```python
import jax
import jax.numpy as jnp
from jax import lax
from jax.sharding import PartitionSpec as P


def per_device(tokens, expert_ids, slot_ids, router, w_in, w_out):
    tok_rows, width_model = tokens.shape
    experts = router.shape[1]
    capacity = 5 * tok_rows // (4 * experts)
    expert_hit = expert_ids[None, :] == jnp.arange(experts, dtype=jnp.int32)[:, None]
    onehots = [
        (expert_hit & (slot_ids[None, :] == c)).astype(jnp.bfloat16) for c in range(capacity)
    ]
    dispatch = jnp.concatenate(
        [
            jnp.dot(oh, tokens, preferred_element_type=jnp.float32).astype(jnp.bfloat16)
            for oh in onehots
        ],
        axis=1,
    )
    inward = w_in[0]
    outward = w_out[0]
    routed = lax.all_to_all(dispatch, "expert", split_axis=0, concat_axis=0, tiled=True)
    arrived = lax.all_gather(routed, "section", axis=0, tiled=True)
    outs = []
    for c in range(capacity):
        rows = arrived[:, c * width_model : (c + 1) * width_model]
        hidden = jax.nn.relu(
            jnp.dot(rows, inward, preferred_element_type=jnp.float32)
        ).astype(jnp.bfloat16)
        outs.append(
            jnp.dot(hidden, outward, preferred_element_type=jnp.float32).astype(jnp.bfloat16)
        )
    summed = lax.psum_scatter(
        jnp.concatenate(outs, axis=1), "section", scatter_dimension=0, tiled=True
    )
    returned = lax.all_to_all(summed, "expert", split_axis=0, concat_axis=0, tiled=True)
    combined = None
    for c in range(capacity):
        piece = lax.dot_general(
            onehots[c],
            returned[:, c * width_model : (c + 1) * width_model],
            (((0,), (0,)), ((), ())),
            preferred_element_type=jnp.float32,
        )
        combined = piece if combined is None else combined + piece
    logits = jnp.dot(tokens, router, preferred_element_type=jnp.float32)
    gating = jax.nn.sigmoid(
        jnp.sum(jnp.where(expert_hit.T, logits, jnp.zeros_like(logits)), axis=1)
    )
    return (gating[:, None] * combined).astype(jnp.bfloat16)


def solution(mesh):
    return jax.shard_map(
        per_device,
        mesh=mesh,
        in_specs=(
            P(("section", "expert"), None),
            P(("section", "expert")),
            P(("section", "expert")),
            P(),
            P("expert", None, "section"),
            P("expert", "section", None),
        ),
        out_specs=P(("section", "expert"), None),
        check_vma=False,
    )
```

```python
import jax
import jax.numpy as jnp
from jax import lax
from jax.sharding import PartitionSpec as P


def _neighbour_perms(n_sec):
    row = n_sec // 2
    right = [(s, (s // row) * row + (s % row + 1) % row) for s in range(n_sec)]
    left = [(s, (s // row) * row + (s % row - 1) % row) for s in range(n_sec)]
    partner = [(s, (s + row) % n_sec) for s in range(n_sec)]
    return right, left, partner


def _halves(a):
    h = a.shape[0] // 2
    return a[:h], a[h:]


def _section_gather(mine, perms):
    right, left, partner = perms
    pp = lambda v, p: lax.ppermute(v, "section", p)
    b = pp(mine, right)
    c = pp(mine, left)
    a = pp(mine, partner)
    ap, aq = _halves(a)
    bp, _ = _halves(b)
    _, cq = _halves(c)
    from_left = pp(jnp.concatenate([aq, bp]), right)
    from_right = pp(jnp.concatenate([ap, cq]), left)
    from_partner = pp(jnp.concatenate([bp, cq]), partner)
    h = mine.shape[0] // 2
    lbar = jnp.concatenate([from_partner[:h], from_left[:h]])
    rbar = jnp.concatenate([from_right[:h], from_partner[h:]])
    far = jnp.concatenate([from_left[h:], from_right[h:]])
    farbar = jnp.concatenate([pp(from_partner[:h], right), pp(from_partner[h:], left)])
    return mine, b, c, a, lbar, rbar, far, farbar


def _section_reduce(parts, perms):
    right, left, partner = perms
    pp = lambda v, p: lax.ppermute(v, "section", p)
    f32 = lambda v: v.astype(jnp.float32)
    bf = lambda v: v.astype(jnp.bfloat16)
    pm, pb, pc, pa, plbar, prbar, pfar, pfarbar = parts
    h = pm.shape[0] // 2
    lbar_p = f32(plbar[:h]) + f32(pp(pfarbar[:h], left))
    rbar_q = f32(prbar[h:]) + f32(pp(pfarbar[h:], right))
    to_left = jnp.concatenate([plbar[h:], pfar[:h]])
    to_right = jnp.concatenate([prbar[:h], pfar[h:]])
    to_partner = jnp.concatenate([bf(lbar_p), bf(rbar_q)])
    got_right = f32(pp(to_left, left))
    got_left = f32(pp(to_right, right))
    got_partner = f32(pp(to_partner, partner))
    pa_sum = f32(pa) + jnp.concatenate([got_left[:h], got_right[:h]])
    pb_sum = f32(pb) + jnp.concatenate(
        [got_right[h:] + got_partner[:h], jnp.zeros_like(got_right[h:])]
    )
    pc_sum = f32(pc) + jnp.concatenate(
        [jnp.zeros_like(got_left[h:]), got_left[h:] + got_partner[h:]]
    )
    total = (
        f32(pm)
        + f32(pp(bf(pb_sum), left))
        + f32(pp(bf(pc_sum), right))
        + f32(pp(bf(pa_sum), partner))
    )
    return bf(total)


def per_device(n_sec, tokens, expert_ids, slot_ids, router, w_in, w_out):
    tok_rows, width_model = tokens.shape
    experts = router.shape[1]
    capacity = 5 * tok_rows // (4 * experts)
    perms = _neighbour_perms(n_sec)
    expert_hit = expert_ids[None, :] == jnp.arange(experts, dtype=jnp.int32)[:, None]
    onehots = [
        (expert_hit & (slot_ids[None, :] == c)).astype(jnp.bfloat16) for c in range(capacity)
    ]
    dispatch = jnp.concatenate(
        [
            jnp.dot(oh, tokens, preferred_element_type=jnp.float32).astype(jnp.bfloat16)
            for oh in onehots
        ],
        axis=1,
    )
    inward = w_in[0]
    outward = w_out[0]
    routed = lax.all_to_all(dispatch, "expert", split_axis=0, concat_axis=0, tiled=True)
    shards = _section_gather(routed, perms)

    def expert_ffn(rows_all):
        outs = []
        for c in range(capacity):
            rows = rows_all[:, c * width_model : (c + 1) * width_model]
            hidden = jax.nn.relu(
                jnp.dot(rows, inward, preferred_element_type=jnp.float32)
            ).astype(jnp.bfloat16)
            outs.append(
                jnp.dot(hidden, outward, preferred_element_type=jnp.float32).astype(
                    jnp.bfloat16
                )
            )
        return jnp.concatenate(outs, axis=1)

    n = routed.shape[0]
    near = expert_ffn(jnp.concatenate(shards[:4]))
    away = expert_ffn(jnp.concatenate(shards[4:]))
    parts = [near[i * n : (i + 1) * n] for i in range(4)] + [
        away[i * n : (i + 1) * n] for i in range(4)
    ]
    summed = _section_reduce(parts, perms)
    returned = lax.all_to_all(summed, "expert", split_axis=0, concat_axis=0, tiled=True)
    combined = None
    for c in range(capacity):
        piece = lax.dot_general(
            onehots[c],
            returned[:, c * width_model : (c + 1) * width_model],
            (((0,), (0,)), ((), ())),
            preferred_element_type=jnp.float32,
        )
        combined = piece if combined is None else combined + piece
    logits = jnp.dot(tokens, router, preferred_element_type=jnp.float32)
    gating = jax.nn.sigmoid(
        jnp.sum(jnp.where(expert_hit.T, logits, jnp.zeros_like(logits)), axis=1)
    )
    return (gating[:, None] * combined).astype(jnp.bfloat16)


def solution(mesh):
    n_sec = mesh.shape["section"]
    return jax.shard_map(
        lambda *args: per_device(n_sec, *args),
        mesh=mesh,
        in_specs=(
            P(("section", "expert"), None),
            P(("section", "expert")),
            P(("section", "expert")),
            P(),
            P("expert", None, "section"),
            P("expert", "section", None),
        ),
        out_specs=P(("section", "expert"), None),
        check_vma=False,
    )
```

```python
import jax
import jax.numpy as jnp
from jax import lax
from jax.sharding import PartitionSpec as P


def _neighbour_perms(n_sec):
    row = n_sec // 2
    right = [(s, (s // row) * row + (s % row + 1) % row) for s in range(n_sec)]
    left = [(s, (s // row) * row + (s % row - 1) % row) for s in range(n_sec)]
    partner = [(s, (s + row) % n_sec) for s in range(n_sec)]
    return right, left, partner


def _halves(a):
    h = a.shape[0] // 2
    return a[:h], a[h:]


def _section_gather(mine, perms):
    right, left, partner = perms
    pp = lambda v, p: lax.ppermute(v, "section", p)
    b = pp(mine, right)
    c = pp(mine, left)
    a = pp(mine, partner)
    ap, aq = _halves(a)
    bp, _ = _halves(b)
    _, cq = _halves(c)
    from_left = pp(jnp.concatenate([aq, bp]), right)
    from_right = pp(jnp.concatenate([ap, cq]), left)
    from_partner = pp(jnp.concatenate([bp, cq]), partner)
    h = mine.shape[0] // 2
    lbar = jnp.concatenate([from_partner[:h], from_left[:h]])
    rbar = jnp.concatenate([from_right[:h], from_partner[h:]])
    far = jnp.concatenate([from_left[h:], from_right[h:]])
    farbar = jnp.concatenate([pp(from_partner[:h], right), pp(from_partner[h:], left)])
    return mine, b, c, a, lbar, rbar, far, farbar


def _section_reduce(parts, perms):
    right, left, partner = perms
    pp = lambda v, p: lax.ppermute(v, "section", p)
    f32 = lambda v: v.astype(jnp.float32)
    bf = lambda v: v.astype(jnp.bfloat16)
    pm, pb, pc, pa, plbar, prbar, pfar, pfarbar = parts
    h = pm.shape[0] // 2
    lbar_p = f32(plbar[:h]) + f32(pp(pfarbar[:h], left))
    rbar_q = f32(prbar[h:]) + f32(pp(pfarbar[h:], right))
    to_left = jnp.concatenate([plbar[h:], pfar[:h]])
    to_right = jnp.concatenate([prbar[:h], pfar[h:]])
    to_partner = jnp.concatenate([bf(lbar_p), bf(rbar_q)])
    got_right = f32(pp(to_left, left))
    got_left = f32(pp(to_right, right))
    got_partner = f32(pp(to_partner, partner))
    pa_sum = f32(pa) + jnp.concatenate([got_left[:h], got_right[:h]])
    pb_sum = f32(pb) + jnp.concatenate(
        [got_right[h:] + got_partner[:h], jnp.zeros_like(got_right[h:])]
    )
    pc_sum = f32(pc) + jnp.concatenate(
        [jnp.zeros_like(got_left[h:]), got_left[h:] + got_partner[h:]]
    )
    total = (
        f32(pm)
        + f32(pp(bf(pb_sum), left))
        + f32(pp(bf(pc_sum), right))
        + f32(pp(bf(pa_sum), partner))
    )
    return bf(total)


def per_device(n_sec, tokens, expert_ids, slot_ids, router, w_in, w_out):
    tok_rows, width_model = tokens.shape
    experts = router.shape[1]
    capacity = 5 * tok_rows // (4 * experts)
    perms = _neighbour_perms(n_sec)
    expert_hit = expert_ids[None, :] == jnp.arange(experts, dtype=jnp.int32)[:, None]
    onehots = [
        (expert_hit & (slot_ids[None, :] == c)).astype(jnp.bfloat16) for c in range(capacity)
    ]
    dispatch = jnp.concatenate(
        [
            jnp.dot(oh, tokens, preferred_element_type=jnp.float32).astype(jnp.bfloat16)
            for oh in onehots
        ],
        axis=1,
    )
    inward = w_in[0]
    outward = w_out[0]
    routed = lax.all_to_all(dispatch, "expert", split_axis=0, concat_axis=0, tiled=True)
    shards = _section_gather(routed, perms)

    def expert_ffn(rows_all):
        outs = []
        for c in range(capacity):
            rows = rows_all[:, c * width_model : (c + 1) * width_model]
            hidden = jax.nn.relu(
                jnp.dot(rows, inward, preferred_element_type=jnp.float32)
            ).astype(jnp.bfloat16)
            hidden = lax.optimization_barrier(hidden)
            outs.append(
                jnp.dot(hidden, outward, preferred_element_type=jnp.float32).astype(
                    jnp.bfloat16
                )
            )
        return jnp.concatenate(outs, axis=1)

    n = routed.shape[0]
    near = expert_ffn(jnp.concatenate(shards[:4]))
    away = expert_ffn(jnp.concatenate(shards[4:]))
    parts = [near[i * n : (i + 1) * n] for i in range(4)] + [
        away[i * n : (i + 1) * n] for i in range(4)
    ]
    summed = _section_reduce(parts, perms)
    returned = lax.all_to_all(summed, "expert", split_axis=0, concat_axis=0, tiled=True)
    combined = None
    for c in range(capacity):
        piece = lax.dot_general(
            onehots[c],
            returned[:, c * width_model : (c + 1) * width_model],
            (((0,), (0,)), ((), ())),
            preferred_element_type=jnp.float32,
        )
        combined = piece if combined is None else combined + piece
    logits = jnp.dot(tokens, router, preferred_element_type=jnp.float32)
    gating = jax.nn.sigmoid(
        jnp.sum(jnp.where(expert_hit.T, logits, jnp.zeros_like(logits)), axis=1)
    )
    return (gating[:, None] * combined).astype(jnp.bfloat16)


def solution(mesh):
    n_sec = mesh.shape["section"]
    return jax.shard_map(
        lambda *args: per_device(n_sec, *args),
        mesh=mesh,
        in_specs=(
            P(("section", "expert"), None),
            P(("section", "expert")),
            P(("section", "expert")),
            P(),
            P("expert", None, "section"),
            P("expert", "section", None),
        ),
        out_specs=P(("section", "expert"), None),
        check_vma=False,
    )
```

```python
import jax
import jax.numpy as jnp
from jax import lax
from jax.sharding import PartitionSpec as P


def _neighbour_perms(n_sec):
    row = n_sec // 2
    right = [(s, (s // row) * row + (s % row + 1) % row) for s in range(n_sec)]
    left = [(s, (s // row) * row + (s % row - 1) % row) for s in range(n_sec)]
    partner = [(s, (s + row) % n_sec) for s in range(n_sec)]
    return right, left, partner


def _halves(a):
    h = a.shape[0] // 2
    return a[:h], a[h:]


def _section_gather(mine, perms):
    right, left, partner = perms
    pp = lambda v, p: lax.ppermute(v, "section", p)
    b = pp(mine, right)
    c = pp(mine, left)
    a = pp(mine, partner)
    ap, aq = _halves(a)
    bp, _ = _halves(b)
    _, cq = _halves(c)
    from_left = pp(jnp.concatenate([aq, bp]), right)
    from_right = pp(jnp.concatenate([ap, cq]), left)
    from_partner = pp(jnp.concatenate([bp, cq]), partner)
    h = mine.shape[0] // 2
    lbar = jnp.concatenate([from_partner[:h], from_left[:h]])
    rbar = jnp.concatenate([from_right[:h], from_partner[h:]])
    far = jnp.concatenate([from_left[h:], from_right[h:]])
    farbar = jnp.concatenate([pp(from_partner[:h], right), pp(from_partner[h:], left)])
    return mine, b, c, a, lbar, rbar, far, farbar


def _section_reduce(parts, perms):
    right, left, partner = perms
    pp = lambda v, p: lax.ppermute(v, "section", p)
    f32 = lambda v: v.astype(jnp.float32)
    bf = lambda v: v.astype(jnp.bfloat16)
    pm, pb, pc, pa, plbar, prbar, pfar, pfarbar = parts
    h = pm.shape[0] // 2
    lbar_p = f32(plbar[:h]) + f32(pp(pfarbar[:h], left))
    rbar_q = f32(prbar[h:]) + f32(pp(pfarbar[h:], right))
    to_left = jnp.concatenate([plbar[h:], pfar[:h]])
    to_right = jnp.concatenate([prbar[:h], pfar[h:]])
    to_partner = jnp.concatenate([bf(lbar_p), bf(rbar_q)])
    got_right = f32(pp(to_left, left))
    got_left = f32(pp(to_right, right))
    got_partner = f32(pp(to_partner, partner))
    pa_sum = f32(pa) + jnp.concatenate([got_left[:h], got_right[:h]])
    pb_sum = f32(pb) + jnp.concatenate(
        [got_right[h:] + got_partner[:h], jnp.zeros_like(got_right[h:])]
    )
    pc_sum = f32(pc) + jnp.concatenate(
        [jnp.zeros_like(got_left[h:]), got_left[h:] + got_partner[h:]]
    )
    total = (
        f32(pm)
        + f32(pp(bf(pb_sum), left))
        + f32(pp(bf(pc_sum), right))
        + f32(pp(bf(pa_sum), partner))
    )
    return bf(total)


def per_device(n_sec, tokens, expert_ids, slot_ids, router, w_in, w_out):
    tok_rows, width_model = tokens.shape
    experts = router.shape[1]
    capacity = 5 * tok_rows // (4 * experts)
    perms = _neighbour_perms(n_sec)
    expert_hit = expert_ids[None, :] == jnp.arange(experts, dtype=jnp.int32)[:, None]
    onehots = [
        (expert_hit & (slot_ids[None, :] == c)).astype(jnp.bfloat16) for c in range(capacity)
    ]
    inward = w_in[0]
    outward = w_out[0]
    first = (capacity + 1) // 2 - 1 if capacity > 2 else 1
    chains = [list(range(0, first + 1)), list(range(first + 1, capacity))]
    chains = [c for c in chains if c]

    def expert_ffn(rows_all, count):
        outs = []
        for c in range(count):
            rows = rows_all[:, c * width_model : (c + 1) * width_model]
            hidden = jax.nn.relu(
                jnp.dot(rows, inward, preferred_element_type=jnp.float32)
            ).astype(jnp.bfloat16)
            hidden = lax.optimization_barrier(hidden)
            outs.append(
                jnp.dot(hidden, outward, preferred_element_type=jnp.float32).astype(
                    jnp.bfloat16
                )
            )
        return jnp.concatenate(outs, axis=1)

    combined = None
    for slots in chains:
        dispatch = jnp.concatenate(
            [
                jnp.dot(onehots[c], tokens, preferred_element_type=jnp.float32).astype(
                    jnp.bfloat16
                )
                for c in slots
            ],
            axis=1,
        )
        routed = lax.all_to_all(dispatch, "expert", split_axis=0, concat_axis=0, tiled=True)
        shards = _section_gather(routed, perms)
        n = routed.shape[0]
        near = expert_ffn(jnp.concatenate(shards[:4]), len(slots))
        away = expert_ffn(jnp.concatenate(shards[4:]), len(slots))
        parts = [near[i * n : (i + 1) * n] for i in range(4)] + [
            away[i * n : (i + 1) * n] for i in range(4)
        ]
        summed = _section_reduce(parts, perms)
        returned = lax.all_to_all(summed, "expert", split_axis=0, concat_axis=0, tiled=True)
        for j, c in enumerate(slots):
            piece = lax.dot_general(
                onehots[c],
                returned[:, j * width_model : (j + 1) * width_model],
                (((0,), (0,)), ((), ())),
                preferred_element_type=jnp.float32,
            )
            combined = piece if combined is None else combined + piece
    logits = jnp.dot(tokens, router, preferred_element_type=jnp.float32)
    gating = jax.nn.sigmoid(
        jnp.sum(jnp.where(expert_hit.T, logits, jnp.zeros_like(logits)), axis=1)
    )
    return (gating[:, None] * combined).astype(jnp.bfloat16)


def solution(mesh):
    n_sec = mesh.shape["section"]
    return jax.shard_map(
        lambda *args: per_device(n_sec, *args),
        mesh=mesh,
        in_specs=(
            P(("section", "expert"), None),
            P(("section", "expert")),
            P(("section", "expert")),
            P(),
            P("expert", None, "section"),
            P("expert", "section", None),
        ),
        out_specs=P(("section", "expert"), None),
        check_vma=False,
    )
```

```python
import jax
import jax.numpy as jnp
from jax import lax
from jax.sharding import PartitionSpec as P


def _neighbour_perms(n_sec):
    row = n_sec // 2
    right = [(s, (s // row) * row + (s % row + 1) % row) for s in range(n_sec)]
    left = [(s, (s // row) * row + (s % row - 1) % row) for s in range(n_sec)]
    partner = [(s, (s + row) % n_sec) for s in range(n_sec)]
    return right, left, partner


def _halves(a):
    h = a.shape[0] // 2
    return a[:h], a[h:]


def _section_gather(mine, perms):
    right, left, partner = perms
    pp = lambda v, p: lax.ppermute(v, "section", p)
    b = pp(mine, right)
    c = pp(mine, left)
    a = pp(mine, partner)
    ap, aq = _halves(a)
    bp, _ = _halves(b)
    _, cq = _halves(c)
    from_left = pp(jnp.concatenate([aq, bp]), right)
    from_right = pp(jnp.concatenate([ap, cq]), left)
    from_partner = pp(jnp.concatenate([bp, cq]), partner)
    h = mine.shape[0] // 2
    lbar = jnp.concatenate([from_partner[:h], from_left[:h]])
    rbar = jnp.concatenate([from_right[:h], from_partner[h:]])
    far = jnp.concatenate([from_left[h:], from_right[h:]])
    farbar = jnp.concatenate([pp(from_partner[:h], right), pp(from_partner[h:], left)])
    return mine, b, c, a, lbar, rbar, far, farbar


def _section_reduce(parts, perms, dep=None):
    right, left, partner = perms
    pp = lambda v, p: lax.ppermute(v, "section", p)
    f32 = lambda v: v.astype(jnp.float32)
    bf = lambda v: v.astype(jnp.bfloat16)
    pm, pb, pc, pa, plbar, prbar, pfar, pfarbar = parts
    h = pm.shape[0] // 2
    lbar_p = f32(plbar[:h]) + f32(pp(pfarbar[:h], left))
    rbar_q = f32(prbar[h:]) + f32(pp(pfarbar[h:], right))
    to_left = jnp.concatenate([plbar[h:], pfar[:h]])
    to_right = jnp.concatenate([prbar[:h], pfar[h:]])
    to_partner = jnp.concatenate([bf(lbar_p), bf(rbar_q)])
    got_right = f32(pp(to_left, left))
    got_left = f32(pp(to_right, right))
    got_partner = f32(pp(to_partner, partner))
    pa_sum = f32(pa) + jnp.concatenate([got_left[:h], got_right[:h]])
    pb_sum = f32(pb) + jnp.concatenate(
        [got_right[h:] + got_partner[:h], jnp.zeros_like(got_right[h:])]
    )
    pc_sum = f32(pc) + jnp.concatenate(
        [jnp.zeros_like(got_left[h:]), got_left[h:] + got_partner[h:]]
    )
    if dep is not None:
        (pa_sum, pb_sum, pc_sum), _ = lax.optimization_barrier(((pa_sum, pb_sum, pc_sum), dep))
    total = (
        f32(pm)
        + f32(pp(bf(pb_sum), left))
        + f32(pp(bf(pc_sum), right))
        + f32(pp(bf(pa_sum), partner))
    )
    return bf(total)


def per_device(n_sec, tokens, expert_ids, slot_ids, router, w_in, w_out):
    tok_rows, width_model = tokens.shape
    experts = router.shape[1]
    capacity = 5 * tok_rows // (4 * experts)
    perms = _neighbour_perms(n_sec)
    expert_hit = expert_ids[None, :] == jnp.arange(experts, dtype=jnp.int32)[:, None]
    onehots = [
        (expert_hit & (slot_ids[None, :] == c)).astype(jnp.bfloat16) for c in range(capacity)
    ]
    inward = w_in[0]
    outward = w_out[0]
    chains = [[0], list(range(1, capacity - 1)), [capacity - 1]]
    chains = [c for c in chains if c]

    def expert_ffn(rows_all, count):
        outs = []
        for c in range(count):
            rows = rows_all[:, c * width_model : (c + 1) * width_model]
            hidden = jax.nn.relu(
                jnp.dot(rows, inward, preferred_element_type=jnp.float32)
            ).astype(jnp.bfloat16)
            hidden = lax.optimization_barrier(hidden)
            outs.append(
                jnp.dot(hidden, outward, preferred_element_type=jnp.float32).astype(
                    jnp.bfloat16
                )
            )
        return jnp.concatenate(outs, axis=1)

    combined = None
    prev_summed = None
    prev_returned = None
    for k, slots in enumerate(chains):
        dispatch = jnp.concatenate(
            [
                jnp.dot(onehots[c], tokens, preferred_element_type=jnp.float32).astype(
                    jnp.bfloat16
                )
                for c in slots
            ],
            axis=1,
        )
        routed = lax.all_to_all(dispatch, "expert", split_axis=0, concat_axis=0, tiled=True)
        shards = _section_gather(routed, perms)
        n = routed.shape[0]
        near = expert_ffn(jnp.concatenate(shards[:4]), len(slots))
        away = expert_ffn(jnp.concatenate(shards[4:]), len(slots))
        parts = [near[i * n : (i + 1) * n] for i in range(4)] + [
            away[i * n : (i + 1) * n] for i in range(4)
        ]
        if k == len(chains) - 1 and prev_summed is not None:
            parts, prev_summed = lax.optimization_barrier((parts, prev_summed))
        last = k == len(chains) - 1
        summed = _section_reduce(parts, perms, prev_returned if last else None)
        prev_summed = summed
        returned = lax.all_to_all(summed, "expert", split_axis=0, concat_axis=0, tiled=True)
        prev_returned = returned
        for j, c in enumerate(slots):
            piece = lax.dot_general(
                onehots[c],
                returned[:, j * width_model : (j + 1) * width_model],
                (((0,), (0,)), ((), ())),
                preferred_element_type=jnp.float32,
            )
            combined = piece if combined is None else combined + piece
    logits = jnp.dot(tokens, router, preferred_element_type=jnp.float32)
    gating = jax.nn.sigmoid(
        jnp.sum(jnp.where(expert_hit.T, logits, jnp.zeros_like(logits)), axis=1)
    )
    return (gating[:, None] * combined).astype(jnp.bfloat16)


def solution(mesh):
    n_sec = mesh.shape["section"]
    return jax.shard_map(
        lambda *args: per_device(n_sec, *args),
        mesh=mesh,
        in_specs=(
            P(("section", "expert"), None),
            P(("section", "expert")),
            P(("section", "expert")),
            P(),
            P("expert", None, "section"),
            P("expert", "section", None),
        ),
        out_specs=P(("section", "expert"), None),
        check_vma=False,
    )
```

```python
import jax
import jax.numpy as jnp
from jax import lax
from jax.sharding import PartitionSpec as P


def _neighbour_perms(n_sec):
    row = n_sec // 2
    right = [(s, (s // row) * row + (s % row + 1) % row) for s in range(n_sec)]
    left = [(s, (s // row) * row + (s % row - 1) % row) for s in range(n_sec)]
    partner = [(s, (s + row) % n_sec) for s in range(n_sec)]
    return right, left, partner


def _halves(a):
    h = a.shape[0] // 2
    return a[:h], a[h:]


def _section_gather(mine, perms):
    right, left, partner = perms
    pp = lambda v, p: lax.ppermute(v, "section", p)
    b = pp(mine, right)
    c = pp(mine, left)
    a = pp(mine, partner)
    ap, aq = _halves(a)
    bp, _ = _halves(b)
    _, cq = _halves(c)
    from_left = pp(jnp.concatenate([aq, bp]), right)
    from_right = pp(jnp.concatenate([ap, cq]), left)
    from_partner = pp(jnp.concatenate([bp, cq]), partner)
    h = mine.shape[0] // 2
    lbar = jnp.concatenate([from_partner[:h], from_left[:h]])
    rbar = jnp.concatenate([from_right[:h], from_partner[h:]])
    far = jnp.concatenate([from_left[h:], from_right[h:]])
    farbar = jnp.concatenate([pp(from_partner[:h], right), pp(from_partner[h:], left)])
    return mine, b, c, a, lbar, rbar, far, farbar


def _section_reduce(parts, perms, dep=None):
    right, left, partner = perms
    pp = lambda v, p: lax.ppermute(v, "section", p)
    f32 = lambda v: v.astype(jnp.float32)
    bf = lambda v: v.astype(jnp.bfloat16)
    pm, pb, pc, pa, plbar, prbar, pfar, pfarbar = parts
    h = pm.shape[0] // 2
    lbar_p = f32(plbar[:h]) + f32(pp(pfarbar[:h], left))
    rbar_q = f32(prbar[h:]) + f32(pp(pfarbar[h:], right))
    to_left = jnp.concatenate([plbar[h:], pfar[:h]])
    to_right = jnp.concatenate([prbar[:h], pfar[h:]])
    to_partner = jnp.concatenate([bf(lbar_p), bf(rbar_q)])
    got_right = f32(pp(to_left, left))
    got_left = f32(pp(to_right, right))
    got_partner = f32(pp(to_partner, partner))
    pa_sum = f32(pa) + jnp.concatenate([got_left[:h], got_right[:h]])
    pb_sum = f32(pb) + jnp.concatenate(
        [got_right[h:] + got_partner[:h], jnp.zeros_like(got_right[h:])]
    )
    pc_sum = f32(pc) + jnp.concatenate(
        [jnp.zeros_like(got_left[h:]), got_left[h:] + got_partner[h:]]
    )
    if dep is not None:
        (pa_sum, pb_sum, pc_sum), _ = lax.optimization_barrier(((pa_sum, pb_sum, pc_sum), dep))
    total = (
        f32(pm)
        + f32(pp(bf(pb_sum), left))
        + f32(pp(bf(pc_sum), right))
        + f32(pp(bf(pa_sum), partner))
    )
    return bf(total)


def per_device(n_sec, tokens, expert_ids, slot_ids, router, w_in, w_out):
    tok_rows, width_model = tokens.shape
    experts = router.shape[1]
    capacity = 5 * tok_rows // (4 * experts)
    perms = _neighbour_perms(n_sec)
    expert_hit = expert_ids[None, :] == jnp.arange(experts, dtype=jnp.int32)[:, None]
    onehots = [
        (expert_hit & (slot_ids[None, :] == c)).astype(jnp.bfloat16) for c in range(capacity)
    ]
    inward = w_in[0]
    outward = w_out[0]
    first = (capacity + 1) // 2
    chains = [list(range(0, first)), list(range(first, capacity))]
    chains = [c for c in chains if c]

    def expert_ffn(rows_all, count):
        outs = []
        for c in range(count):
            rows = rows_all[:, c * width_model : (c + 1) * width_model]
            hidden = jax.nn.relu(
                jnp.dot(rows, inward, preferred_element_type=jnp.float32)
            ).astype(jnp.bfloat16)
            hidden = lax.optimization_barrier(hidden)
            outs.append(
                jnp.dot(hidden, outward, preferred_element_type=jnp.float32).astype(
                    jnp.bfloat16
                )
            )
        return jnp.concatenate(outs, axis=1)

    combined = None
    prev_summed = None
    prev_returned = None
    for k, slots in enumerate(chains):
        dispatch = jnp.concatenate(
            [
                jnp.dot(onehots[c], tokens, preferred_element_type=jnp.float32).astype(
                    jnp.bfloat16
                )
                for c in slots
            ],
            axis=1,
        )
        routed = lax.all_to_all(dispatch, "expert", split_axis=0, concat_axis=0, tiled=True)
        shards = _section_gather(routed, perms)
        n = routed.shape[0]
        near = expert_ffn(jnp.concatenate(shards[:4]), len(slots))
        away = expert_ffn(jnp.concatenate(shards[4:]), len(slots))
        parts = [near[i * n : (i + 1) * n] for i in range(4)] + [
            away[i * n : (i + 1) * n] for i in range(4)
        ]
        if k == len(chains) - 1 and prev_summed is not None:
            parts, prev_summed = lax.optimization_barrier((parts, prev_summed))
        last = k == len(chains) - 1
        summed = _section_reduce(parts, perms, prev_returned if last else None)
        prev_summed = summed
        returned = lax.all_to_all(summed, "expert", split_axis=0, concat_axis=0, tiled=True)
        prev_returned = returned
        for j, c in enumerate(slots):
            piece = lax.dot_general(
                onehots[c],
                returned[:, j * width_model : (j + 1) * width_model],
                (((0,), (0,)), ((), ())),
                preferred_element_type=jnp.float32,
            )
            combined = piece if combined is None else combined + piece
    logits = jnp.dot(tokens, router, preferred_element_type=jnp.float32)
    gating = jax.nn.sigmoid(
        jnp.sum(jnp.where(expert_hit.T, logits, jnp.zeros_like(logits)), axis=1)
    )
    return (gating[:, None] * combined).astype(jnp.bfloat16)


def solution(mesh):
    n_sec = mesh.shape["section"]
    return jax.shard_map(
        lambda *args: per_device(n_sec, *args),
        mesh=mesh,
        in_specs=(
            P(("section", "expert"), None),
            P(("section", "expert")),
            P(("section", "expert")),
            P(),
            P("expert", None, "section"),
            P("expert", "section", None),
        ),
        out_specs=P(("section", "expert"), None),
        check_vma=False,
    )
```

```python
import jax
import jax.numpy as jnp
from jax import lax
from jax.sharding import PartitionSpec as P


def _neighbour_perms(n_sec):
    row = n_sec // 2
    right = [(s, (s // row) * row + (s % row + 1) % row) for s in range(n_sec)]
    left = [(s, (s // row) * row + (s % row - 1) % row) for s in range(n_sec)]
    partner = [(s, (s + row) % n_sec) for s in range(n_sec)]
    return right, left, partner


def _halves(a):
    h = a.shape[0] // 2
    return a[:h], a[h:]


def _section_gather(mine, perms):
    right, left, partner = perms
    pp = lambda v, p: lax.ppermute(v, "section", p)
    b = pp(mine, right)
    c = pp(mine, left)
    a = pp(mine, partner)
    ap, aq = _halves(a)
    bp, _ = _halves(b)
    _, cq = _halves(c)
    from_left = pp(jnp.concatenate([aq, bp]), right)
    from_right = pp(jnp.concatenate([ap, cq]), left)
    from_partner = pp(jnp.concatenate([bp, cq]), partner)
    h = mine.shape[0] // 2
    lbar = jnp.concatenate([from_partner[:h], from_left[:h]])
    rbar = jnp.concatenate([from_right[:h], from_partner[h:]])
    far = jnp.concatenate([from_left[h:], from_right[h:]])
    farbar = jnp.concatenate([pp(from_partner[:h], right), pp(from_partner[h:], left)])
    return mine, b, c, a, lbar, rbar, far, farbar


def _section_reduce(parts, perms):
    right, left, partner = perms
    pp = lambda v, p: lax.ppermute(v, "section", p)
    f32 = lambda v: v.astype(jnp.float32)
    bf = lambda v: v.astype(jnp.bfloat16)
    pm, pb, pc, pa, plbar, prbar, pfar, pfarbar = parts
    h = pm.shape[0] // 2
    lbar_p = f32(plbar[:h]) + f32(pp(pfarbar[:h], left))
    rbar_q = f32(prbar[h:]) + f32(pp(pfarbar[h:], right))
    to_left = jnp.concatenate([plbar[h:], pfar[:h]])
    to_right = jnp.concatenate([prbar[:h], pfar[h:]])
    to_partner = jnp.concatenate([bf(lbar_p), bf(rbar_q)])
    got_right = f32(pp(to_left, left))
    got_left = f32(pp(to_right, right))
    got_partner = f32(pp(to_partner, partner))
    pa_sum = f32(pa) + jnp.concatenate([got_left[:h], got_right[:h]])
    pb_sum = f32(pb) + jnp.concatenate(
        [got_right[h:] + got_partner[:h], jnp.zeros_like(got_right[h:])]
    )
    pc_sum = f32(pc) + jnp.concatenate(
        [jnp.zeros_like(got_left[h:]), got_left[h:] + got_partner[h:]]
    )
    total = (
        f32(pm)
        + f32(pp(bf(pb_sum), left))
        + f32(pp(bf(pc_sum), right))
        + f32(pp(bf(pa_sum), partner))
    )
    return bf(total)


def per_device(n_sec, tokens, expert_ids, slot_ids, router, w_in, w_out):
    tok_rows, width_model = tokens.shape
    experts = router.shape[1]
    capacity = 5 * tok_rows // (4 * experts)
    perms = _neighbour_perms(n_sec)
    expert_hit = expert_ids[None, :] == jnp.arange(experts, dtype=jnp.int32)[:, None]
    onehots = [
        (expert_hit & (slot_ids[None, :] == c)).astype(jnp.bfloat16) for c in range(capacity)
    ]
    inward = w_in[0]
    outward = w_out[0]
    first = (capacity + 1) // 2 - 1 if capacity > 2 else 1
    chains = [list(range(0, first + 1)), list(range(first + 1, capacity))]
    chains = [c for c in chains if c]

    def expert_ffn(rows_all, count):
        outs = []
        for c in range(count):
            rows = rows_all[:, c, :]
            hidden = jax.nn.relu(
                jnp.dot(rows, inward, preferred_element_type=jnp.float32)
            ).astype(jnp.bfloat16)
            hidden = lax.optimization_barrier(hidden)
            outs.append(
                jnp.dot(hidden, outward, preferred_element_type=jnp.float32).astype(
                    jnp.bfloat16
                )
            )
        return jnp.stack(outs, axis=1)

    combined = None
    for slots in chains:
        dispatch = jnp.stack(
            [
                jnp.dot(onehots[c], tokens, preferred_element_type=jnp.float32).astype(
                    jnp.bfloat16
                )
                for c in slots
            ],
            axis=1,
        )
        routed = lax.all_to_all(dispatch, "expert", split_axis=0, concat_axis=0, tiled=True)
        shards = _section_gather(routed, perms)
        n = routed.shape[0]
        near = expert_ffn(jnp.concatenate(shards[:4]), len(slots))
        away = expert_ffn(jnp.concatenate(shards[4:]), len(slots))
        parts = [near[i * n : (i + 1) * n] for i in range(4)] + [
            away[i * n : (i + 1) * n] for i in range(4)
        ]
        summed = _section_reduce(parts, perms)
        returned = lax.all_to_all(summed, "expert", split_axis=0, concat_axis=0, tiled=True)
        for j, c in enumerate(slots):
            piece = lax.dot_general(
                onehots[c],
                returned[:, j, :],
                (((0,), (0,)), ((), ())),
                preferred_element_type=jnp.float32,
            )
            combined = piece if combined is None else combined + piece
    logits = jnp.dot(tokens, router, preferred_element_type=jnp.float32)
    gating = jax.nn.sigmoid(
        jnp.sum(jnp.where(expert_hit.T, logits, jnp.zeros_like(logits)), axis=1)
    )
    return (gating[:, None] * combined).astype(jnp.bfloat16)


def solution(mesh):
    n_sec = mesh.shape["section"]
    return jax.shard_map(
        lambda *args: per_device(n_sec, *args),
        mesh=mesh,
        in_specs=(
            P(("section", "expert"), None),
            P(("section", "expert")),
            P(("section", "expert")),
            P(),
            P("expert", None, "section"),
            P("expert", "section", None),
        ),
        out_specs=P(("section", "expert"), None),
        check_vma=False,
    )
```

```python
import jax
import jax.numpy as jnp
from jax import lax
from jax.sharding import PartitionSpec as P


def _neighbour_perms(n_sec):
    row = n_sec // 2
    right = [(s, (s // row) * row + (s % row + 1) % row) for s in range(n_sec)]
    left = [(s, (s // row) * row + (s % row - 1) % row) for s in range(n_sec)]
    partner = [(s, (s + row) % n_sec) for s in range(n_sec)]
    return right, left, partner


def _halves(a):
    h = a.shape[0] // 2
    return a[:h], a[h:]


def _section_gather(mine, perms):
    right, left, partner = perms
    pp = lambda v, p: lax.ppermute(v, "section", p)
    b = pp(mine, right)
    c = pp(mine, left)
    a = pp(mine, partner)
    ap, aq = _halves(a)
    bp, _ = _halves(b)
    _, cq = _halves(c)
    from_left = pp(jnp.concatenate([aq, bp]), right)
    from_right = pp(jnp.concatenate([ap, cq]), left)
    from_partner = pp(jnp.concatenate([bp, cq]), partner)
    h = mine.shape[0] // 2
    lbar = jnp.concatenate([from_partner[:h], from_left[:h]])
    rbar = jnp.concatenate([from_right[:h], from_partner[h:]])
    far = jnp.concatenate([from_left[h:], from_right[h:]])
    farbar = jnp.concatenate([pp(from_partner[:h], right), pp(from_partner[h:], left)])
    return mine, b, c, a, lbar, rbar, far, farbar


def _section_reduce(parts, perms):
    right, left, partner = perms
    pp = lambda v, p: lax.ppermute(v, "section", p)
    f32 = lambda v: v.astype(jnp.float32)
    bf = lambda v: v.astype(jnp.bfloat16)
    pm, pb, pc, pa, plbar, prbar, pfar, pfarbar = parts
    h = pm.shape[0] // 2
    lbar_p = f32(plbar[:h]) + f32(pp(pfarbar[:h], left))
    rbar_q = f32(prbar[h:]) + f32(pp(pfarbar[h:], right))
    to_left = jnp.concatenate([plbar[h:], pfar[:h]])
    to_right = jnp.concatenate([prbar[:h], pfar[h:]])
    to_partner = jnp.concatenate([bf(lbar_p), bf(rbar_q)])
    got_right = f32(pp(to_left, left))
    got_left = f32(pp(to_right, right))
    got_partner = f32(pp(to_partner, partner))
    pa_sum = f32(pa) + jnp.concatenate([got_left[:h], got_right[:h]])
    pb_sum = f32(pb) + jnp.concatenate(
        [got_right[h:] + got_partner[:h], jnp.zeros_like(got_right[h:])]
    )
    pc_sum = f32(pc) + jnp.concatenate(
        [jnp.zeros_like(got_left[h:]), got_left[h:] + got_partner[h:]]
    )
    total = (
        f32(pm)
        + f32(pp(bf(pb_sum), left))
        + f32(pp(bf(pc_sum), right))
        + f32(pp(bf(pa_sum), partner))
    )
    return bf(total)


def per_device(n_sec, tokens, expert_ids, slot_ids, router, w_in, w_out):
    tok_rows, width_model = tokens.shape
    experts = router.shape[1]
    capacity = 5 * tok_rows // (4 * experts)
    perms = _neighbour_perms(n_sec)
    expert_hit = expert_ids[None, :] == jnp.arange(experts, dtype=jnp.int32)[:, None]
    onehots = [
        (expert_hit & (slot_ids[None, :] == c)).astype(jnp.bfloat16) for c in range(capacity)
    ]
    inward = w_in[0]
    outward = w_out[0]
    chains = [[0], list(range(1, capacity))]
    chains = [c for c in chains if c]

    def expert_ffn(rows_all, count):
        outs = []
        for c in range(count):
            rows = rows_all[:, c * width_model : (c + 1) * width_model]
            hidden = jax.nn.relu(
                jnp.dot(rows, inward, preferred_element_type=jnp.float32)
            ).astype(jnp.bfloat16)
            hidden = lax.optimization_barrier(hidden)
            outs.append(
                jnp.dot(hidden, outward, preferred_element_type=jnp.float32).astype(
                    jnp.bfloat16
                )
            )
        return jnp.concatenate(outs, axis=1)

    combined = None
    for slots in chains:
        dispatch = jnp.concatenate(
            [
                jnp.dot(onehots[c], tokens, preferred_element_type=jnp.float32).astype(
                    jnp.bfloat16
                )
                for c in slots
            ],
            axis=1,
        )
        routed = lax.all_to_all(dispatch, "expert", split_axis=0, concat_axis=0, tiled=True)
        shards = _section_gather(routed, perms)
        n = routed.shape[0]
        near = expert_ffn(jnp.concatenate(shards[:4]), len(slots))
        away = expert_ffn(jnp.concatenate(shards[4:]), len(slots))
        parts = [near[i * n : (i + 1) * n] for i in range(4)] + [
            away[i * n : (i + 1) * n] for i in range(4)
        ]
        summed = _section_reduce(parts, perms)
        returned = lax.all_to_all(summed, "expert", split_axis=0, concat_axis=0, tiled=True)
        for j, c in enumerate(slots):
            piece = lax.dot_general(
                onehots[c],
                returned[:, j * width_model : (j + 1) * width_model],
                (((0,), (0,)), ((), ())),
                preferred_element_type=jnp.float32,
            )
            combined = piece if combined is None else combined + piece
    logits = jnp.dot(tokens, router, preferred_element_type=jnp.float32)
    gating = jax.nn.sigmoid(
        jnp.sum(jnp.where(expert_hit.T, logits, jnp.zeros_like(logits)), axis=1)
    )
    return (gating[:, None] * combined).astype(jnp.bfloat16)


def solution(mesh):
    n_sec = mesh.shape["section"]
    return jax.shard_map(
        lambda *args: per_device(n_sec, *args),
        mesh=mesh,
        in_specs=(
            P(("section", "expert"), None),
            P(("section", "expert")),
            P(("section", "expert")),
            P(),
            P("expert", None, "section"),
            P("expert", "section", None),
        ),
        out_specs=P(("section", "expert"), None),
        check_vma=False,
    )
```

```python
import jax
import jax.numpy as jnp
from jax import lax
from jax.sharding import PartitionSpec as P


def _neighbour_perms(n_sec):
    row = n_sec // 2
    right = [(s, (s // row) * row + (s % row + 1) % row) for s in range(n_sec)]
    left = [(s, (s // row) * row + (s % row - 1) % row) for s in range(n_sec)]
    partner = [(s, (s + row) % n_sec) for s in range(n_sec)]
    return right, left, partner


def _halves(a):
    h = a.shape[0] // 2
    return a[:h], a[h:]


def _section_gather(mine, perms):
    right, left, partner = perms
    pp = lambda v, p: lax.ppermute(v, "section", p)
    b = pp(mine, right)
    c = pp(mine, left)
    a = pp(mine, partner)
    ap, aq = _halves(a)
    bp, _ = _halves(b)
    _, cq = _halves(c)
    from_left = pp(jnp.concatenate([aq, bp]), right)
    from_right = pp(jnp.concatenate([ap, cq]), left)
    from_partner = pp(jnp.concatenate([bp, cq]), partner)
    h = mine.shape[0] // 2
    lbar = jnp.concatenate([from_partner[:h], from_left[:h]])
    rbar = jnp.concatenate([from_right[:h], from_partner[h:]])
    far = jnp.concatenate([from_left[h:], from_right[h:]])
    farbar = jnp.concatenate([pp(from_partner[:h], right), pp(from_partner[h:], left)])
    return mine, b, c, a, lbar, rbar, far, farbar


def _section_reduce(parts, perms):
    right, left, partner = perms
    pp = lambda v, p: lax.ppermute(v, "section", p)
    f32 = lambda v: v.astype(jnp.float32)
    bf = lambda v: v.astype(jnp.bfloat16)
    pm, pb, pc, pa, plbar, prbar, pfar, pfarbar = parts
    h = pm.shape[0] // 2
    lbar_p = f32(plbar[:h]) + f32(pp(pfarbar[:h], left))
    rbar_q = f32(prbar[h:]) + f32(pp(pfarbar[h:], right))
    to_left = jnp.concatenate([plbar[h:], pfar[:h]])
    to_right = jnp.concatenate([prbar[:h], pfar[h:]])
    to_partner = jnp.concatenate([bf(lbar_p), bf(rbar_q)])
    got_right = f32(pp(to_left, left))
    got_left = f32(pp(to_right, right))
    got_partner = f32(pp(to_partner, partner))
    pa_sum = f32(pa) + jnp.concatenate([got_left[:h], got_right[:h]])
    pb_sum = f32(pb) + jnp.concatenate(
        [got_right[h:] + got_partner[:h], jnp.zeros_like(got_right[h:])]
    )
    pc_sum = f32(pc) + jnp.concatenate(
        [jnp.zeros_like(got_left[h:]), got_left[h:] + got_partner[h:]]
    )
    total = (
        f32(pm)
        + f32(pp(bf(pb_sum), left))
        + f32(pp(bf(pc_sum), right))
        + f32(pp(bf(pa_sum), partner))
    )
    return bf(total)


def per_device(n_sec, tokens, expert_ids, slot_ids, router, w_in, w_out):
    tok_rows, width_model = tokens.shape
    experts = router.shape[1]
    capacity = 5 * tok_rows // (4 * experts)
    perms = _neighbour_perms(n_sec)
    expert_hit = expert_ids[None, :] == jnp.arange(experts, dtype=jnp.int32)[:, None]
    onehots = [
        (expert_hit & (slot_ids[None, :] == c)).astype(jnp.bfloat16) for c in range(capacity)
    ]
    inward = w_in[0]
    outward = w_out[0]
    first = (capacity + 1) // 2 - 1 if capacity > 2 else 1
    chains = [list(range(0, first + 1)), list(range(first + 1, capacity))]
    chains = [c for c in chains if c]

    def expert_ffn(rows_all, count):
        outs = []
        for c in range(count):
            rows = rows_all[:, c * width_model : (c + 1) * width_model]
            hidden = jax.nn.relu(
                jnp.dot(rows, inward, preferred_element_type=jnp.float32)
            ).astype(jnp.bfloat16)
            hidden = lax.optimization_barrier(hidden)
            outs.append(
                jnp.dot(hidden, outward, preferred_element_type=jnp.float32).astype(
                    jnp.bfloat16
                )
            )
        return jnp.concatenate(outs, axis=1)

    combined = None
    reduced = []
    for slots in chains:
        dispatch = jnp.concatenate(
            [
                jnp.dot(onehots[c], tokens, preferred_element_type=jnp.float32).astype(
                    jnp.bfloat16
                )
                for c in slots
            ],
            axis=1,
        )
        routed = lax.all_to_all(dispatch, "expert", split_axis=0, concat_axis=0, tiled=True)
        shards = _section_gather(routed, perms)
        n = routed.shape[0]
        near = expert_ffn(jnp.concatenate(shards[:4]), len(slots))
        away = expert_ffn(jnp.concatenate(shards[4:]), len(slots))
        parts = [near[i * n : (i + 1) * n] for i in range(4)] + [
            away[i * n : (i + 1) * n] for i in range(4)
        ]
        reduced.append(_section_reduce(parts, perms))
    returned = lax.all_to_all(
        jnp.concatenate(reduced, axis=1), "expert", split_axis=0, concat_axis=0, tiled=True
    )
    for j, c in enumerate([c for slots in chains for c in slots]):
        piece = lax.dot_general(
            onehots[c],
            returned[:, j * width_model : (j + 1) * width_model],
            (((0,), (0,)), ((), ())),
            preferred_element_type=jnp.float32,
        )
        combined = piece if combined is None else combined + piece
    logits = jnp.dot(tokens, router, preferred_element_type=jnp.float32)
    gating = jax.nn.sigmoid(
        jnp.sum(jnp.where(expert_hit.T, logits, jnp.zeros_like(logits)), axis=1)
    )
    return (gating[:, None] * combined).astype(jnp.bfloat16)


def solution(mesh):
    n_sec = mesh.shape["section"]
    return jax.shard_map(
        lambda *args: per_device(n_sec, *args),
        mesh=mesh,
        in_specs=(
            P(("section", "expert"), None),
            P(("section", "expert")),
            P(("section", "expert")),
            P(),
            P("expert", None, "section"),
            P("expert", "section", None),
        ),
        out_specs=P(("section", "expert"), None),
        check_vma=False,
    )
```

```python
import jax
import jax.numpy as jnp
from jax import lax
from jax.sharding import PartitionSpec as P


def _neighbour_perms(n_sec):
    row = n_sec // 2
    right = [(s, (s // row) * row + (s % row + 1) % row) for s in range(n_sec)]
    left = [(s, (s // row) * row + (s % row - 1) % row) for s in range(n_sec)]
    partner = [(s, (s + row) % n_sec) for s in range(n_sec)]
    return right, left, partner


def _halves(a):
    h = a.shape[0] // 2
    return a[:h], a[h:]


def _section_gather(mine, perms):
    right, left, partner = perms
    pp = lambda v, p: lax.ppermute(v, "section", p)
    b = pp(mine, right)
    c = pp(mine, left)
    a = pp(mine, partner)
    ap, aq = _halves(a)
    bp, _ = _halves(b)
    _, cq = _halves(c)
    from_left = pp(jnp.concatenate([aq, bp]), right)
    from_right = pp(jnp.concatenate([ap, cq]), left)
    from_partner = pp(jnp.concatenate([bp, cq]), partner)
    h = mine.shape[0] // 2
    lbar = jnp.concatenate([from_partner[:h], from_left[:h]])
    rbar = jnp.concatenate([from_right[:h], from_partner[h:]])
    far = jnp.concatenate([from_left[h:], from_right[h:]])
    farbar = jnp.concatenate([pp(from_partner[:h], right), pp(from_partner[h:], left)])
    return mine, b, c, a, lbar, rbar, far, farbar


def _section_reduce(parts, perms, dep=None):
    right, left, partner = perms
    pp = lambda v, p: lax.ppermute(v, "section", p)
    f32 = lambda v: v.astype(jnp.float32)
    bf = lambda v: v.astype(jnp.bfloat16)
    pm, pb, pc, pa, plbar, prbar, pfar, pfarbar = parts
    h = pm.shape[0] // 2
    lbar_p = f32(plbar[:h]) + f32(pp(pfarbar[:h], left))
    rbar_q = f32(prbar[h:]) + f32(pp(pfarbar[h:], right))
    to_left = jnp.concatenate([plbar[h:], pfar[:h]])
    to_right = jnp.concatenate([prbar[:h], pfar[h:]])
    to_partner = jnp.concatenate([bf(lbar_p), bf(rbar_q)])
    got_right = f32(pp(to_left, left))
    got_left = f32(pp(to_right, right))
    got_partner = f32(pp(to_partner, partner))
    pa_sum = f32(pa) + jnp.concatenate([got_left[:h], got_right[:h]])
    pb_sum = f32(pb) + jnp.concatenate(
        [got_right[h:] + got_partner[:h], jnp.zeros_like(got_right[h:])]
    )
    pc_sum = f32(pc) + jnp.concatenate(
        [jnp.zeros_like(got_left[h:]), got_left[h:] + got_partner[h:]]
    )
    if dep is not None:
        (pa_sum, pb_sum, pc_sum), _ = lax.optimization_barrier(((pa_sum, pb_sum, pc_sum), dep))
    total = (
        f32(pm)
        + f32(pp(bf(pb_sum), left))
        + f32(pp(bf(pc_sum), right))
        + f32(pp(bf(pa_sum), partner))
    )
    return bf(total)


def per_device(n_sec, tokens, expert_ids, slot_ids, router, w_in, w_out):
    tok_rows, width_model = tokens.shape
    experts = router.shape[1]
    capacity = 5 * tok_rows // (4 * experts)
    perms = _neighbour_perms(n_sec)
    expert_hit = expert_ids[None, :] == jnp.arange(experts, dtype=jnp.int32)[:, None]
    onehots = [
        (expert_hit & (slot_ids[None, :] == c)).astype(jnp.bfloat16) for c in range(capacity)
    ]
    inward = w_in[0]
    outward = w_out[0]
    first = (capacity + 1) // 2 - 1 if capacity > 2 else 1
    chains = [list(range(first + 1, capacity)), list(range(0, first + 1))]
    chains = [c for c in chains if c]

    def expert_ffn(rows_all, count):
        outs = []
        for c in range(count):
            rows = rows_all[:, c * width_model : (c + 1) * width_model]
            hidden = jax.nn.relu(
                jnp.dot(rows, inward, preferred_element_type=jnp.float32)
            ).astype(jnp.bfloat16)
            hidden = lax.optimization_barrier(hidden)
            outs.append(
                jnp.dot(hidden, outward, preferred_element_type=jnp.float32).astype(
                    jnp.bfloat16
                )
            )
        return jnp.concatenate(outs, axis=1)

    combined = None
    prev_returned = None
    for slots in chains:
        dispatch = jnp.concatenate(
            [
                jnp.dot(onehots[c], tokens, preferred_element_type=jnp.float32).astype(
                    jnp.bfloat16
                )
                for c in slots
            ],
            axis=1,
        )
        routed = lax.all_to_all(dispatch, "expert", split_axis=0, concat_axis=0, tiled=True)
        shards = _section_gather(routed, perms)
        n = routed.shape[0]
        near = expert_ffn(jnp.concatenate(shards[:4]), len(slots))
        away = expert_ffn(jnp.concatenate(shards[4:]), len(slots))
        parts = [near[i * n : (i + 1) * n] for i in range(4)] + [
            away[i * n : (i + 1) * n] for i in range(4)
        ]
        summed = _section_reduce(parts, perms, prev_returned)
        returned = lax.all_to_all(summed, "expert", split_axis=0, concat_axis=0, tiled=True)
        prev_returned = returned
        for j, c in enumerate(slots):
            piece = lax.dot_general(
                onehots[c],
                returned[:, j * width_model : (j + 1) * width_model],
                (((0,), (0,)), ((), ())),
                preferred_element_type=jnp.float32,
            )
            combined = piece if combined is None else combined + piece
    logits = jnp.dot(tokens, router, preferred_element_type=jnp.float32)
    gating = jax.nn.sigmoid(
        jnp.sum(jnp.where(expert_hit.T, logits, jnp.zeros_like(logits)), axis=1)
    )
    return (gating[:, None] * combined).astype(jnp.bfloat16)


def solution(mesh):
    n_sec = mesh.shape["section"]
    return jax.shard_map(
        lambda *args: per_device(n_sec, *args),
        mesh=mesh,
        in_specs=(
            P(("section", "expert"), None),
            P(("section", "expert")),
            P(("section", "expert")),
            P(),
            P("expert", None, "section"),
            P("expert", "section", None),
        ),
        out_specs=P(("section", "expert"), None),
        check_vma=False,
    )
```

```python
import jax
import jax.numpy as jnp
from jax import lax
from jax.sharding import PartitionSpec as P


def _neighbour_perms(n_sec):
    row = n_sec // 2
    right = [(s, (s // row) * row + (s % row + 1) % row) for s in range(n_sec)]
    left = [(s, (s // row) * row + (s % row - 1) % row) for s in range(n_sec)]
    partner = [(s, (s + row) % n_sec) for s in range(n_sec)]
    return right, left, partner


def _halves(a):
    h = a.shape[0] // 2
    return a[:h], a[h:]


def _section_gather(mine, perms):
    right, left, partner = perms
    pp = lambda v, p: lax.ppermute(v, "section", p)
    b = pp(mine, right)
    c = pp(mine, left)
    a = pp(mine, partner)
    ap, aq = _halves(a)
    bp, _ = _halves(b)
    _, cq = _halves(c)
    from_left = pp(jnp.concatenate([aq, bp]), right)
    from_right = pp(jnp.concatenate([ap, cq]), left)
    from_partner = pp(jnp.concatenate([bp, cq]), partner)
    h = mine.shape[0] // 2
    lbar = jnp.concatenate([from_partner[:h], from_left[:h]])
    rbar = jnp.concatenate([from_right[:h], from_partner[h:]])
    far = jnp.concatenate([from_left[h:], from_right[h:]])
    farbar = jnp.concatenate([pp(from_partner[:h], right), pp(from_partner[h:], left)])
    return mine, b, c, a, lbar, rbar, far, farbar


def _section_reduce(parts, perms):
    right, left, partner = perms
    pp = lambda v, p: lax.ppermute(v, "section", p)
    f32 = lambda v: v.astype(jnp.float32)
    bf = lambda v: v.astype(jnp.bfloat16)
    pm, pb, pc, pa, plbar, prbar, pfar, pfarbar = parts
    h = pm.shape[0] // 2
    lbar_p = f32(plbar[:h]) + f32(pp(pfarbar[:h], left))
    rbar_q = f32(prbar[h:]) + f32(pp(pfarbar[h:], right))
    to_left = jnp.concatenate([plbar[h:], pfar[:h]])
    to_right = jnp.concatenate([prbar[:h], pfar[h:]])
    to_partner = jnp.concatenate([bf(lbar_p), bf(rbar_q)])
    got_right = f32(pp(to_left, left))
    got_left = f32(pp(to_right, right))
    got_partner = f32(pp(to_partner, partner))
    pa_sum = bf(f32(pa) + jnp.concatenate([got_left[:h], got_right[:h]]))
    pb_sum = jnp.concatenate([bf(f32(pb[:h]) + got_right[h:] + got_partner[:h]), pb[h:]])
    pc_sum = jnp.concatenate([pc[:h], bf(f32(pc[h:]) + got_left[h:] + got_partner[h:])])
    total = (
        f32(pm)
        + f32(pp(pb_sum, left))
        + f32(pp(pc_sum, right))
        + f32(pp(pa_sum, partner))
    )
    return bf(total)


def per_device(n_sec, tokens, expert_ids, slot_ids, router, w_in, w_out):
    tok_rows, width_model = tokens.shape
    experts = router.shape[1]
    capacity = 5 * tok_rows // (4 * experts)
    perms = _neighbour_perms(n_sec)
    expert_hit = expert_ids[None, :] == jnp.arange(experts, dtype=jnp.int32)[:, None]
    onehots = [
        (expert_hit & (slot_ids[None, :] == c)).astype(jnp.bfloat16) for c in range(capacity)
    ]
    inward = w_in[0]
    outward = w_out[0]
    first = (capacity + 1) // 2 - 1 if capacity > 2 else 1
    chains = [list(range(0, first + 1)), list(range(first + 1, capacity))]
    chains = [c for c in chains if c]

    def expert_ffn(rows_all, count):
        outs = []
        for c in range(count):
            rows = rows_all[:, c * width_model : (c + 1) * width_model]
            hidden = jax.nn.relu(
                jnp.dot(rows, inward, preferred_element_type=jnp.float32)
            ).astype(jnp.bfloat16)
            hidden = lax.optimization_barrier(hidden)
            outs.append(
                jnp.dot(hidden, outward, preferred_element_type=jnp.float32).astype(
                    jnp.bfloat16
                )
            )
        return jnp.concatenate(outs, axis=1)

    combined = None
    for slots in chains:
        dispatch = jnp.concatenate(
            [
                jnp.dot(onehots[c], tokens, preferred_element_type=jnp.float32).astype(
                    jnp.bfloat16
                )
                for c in slots
            ],
            axis=1,
        )
        routed = lax.all_to_all(dispatch, "expert", split_axis=0, concat_axis=0, tiled=True)
        shards = _section_gather(routed, perms)
        n = routed.shape[0]
        near = expert_ffn(jnp.concatenate(shards[:4]), len(slots))
        away = expert_ffn(jnp.concatenate(shards[4:]), len(slots))
        parts = [near[i * n : (i + 1) * n] for i in range(4)] + [
            away[i * n : (i + 1) * n] for i in range(4)
        ]
        summed = _section_reduce(parts, perms)
        returned = lax.all_to_all(summed, "expert", split_axis=0, concat_axis=0, tiled=True)
        for j, c in enumerate(slots):
            piece = lax.dot_general(
                onehots[c],
                returned[:, j * width_model : (j + 1) * width_model],
                (((0,), (0,)), ((), ())),
                preferred_element_type=jnp.float32,
            )
            combined = piece if combined is None else combined + piece
    logits = jnp.dot(tokens, router, preferred_element_type=jnp.float32)
    gating = jax.nn.sigmoid(
        jnp.sum(jnp.where(expert_hit.T, logits, jnp.zeros_like(logits)), axis=1)
    )
    return (gating[:, None] * combined).astype(jnp.bfloat16)


def solution(mesh):
    n_sec = mesh.shape["section"]
    return jax.shard_map(
        lambda *args: per_device(n_sec, *args),
        mesh=mesh,
        in_specs=(
            P(("section", "expert"), None),
            P(("section", "expert")),
            P(("section", "expert")),
            P(),
            P("expert", None, "section"),
            P("expert", "section", None),
        ),
        out_specs=P(("section", "expert"), None),
        check_vma=False,
    )
```
